256 devices in a mesh: lon: 32 (over x_hi, z, core), lat: 8 (over x_lo, y).
Axes of the slice: x: 4 (x_hi: 2, x_lo: 2; x = x_hi * 2 + x_lo), y: 4, z: 8, core: 2. Of those that a mesh axis runs over, the one named last changes fastest.
Arguments:
- tracer_start: float32 [3, 16, 128, 4096], P(None, None, 'lat', 'lon'), may hold values from -6 to 6
- source: float32 [3, 16, 128, 4096], P(None, None, 'lat', 'lon'), may hold values from -3 to 3
- target: float32 [3, 16, 128, 4096], P(None, None, 'lat', 'lon'), may hold values from -27 to 27
- east_vel: float32 [16, 128, 4096], P(None, 'lat', 'lon'), may hold values from -0.12 to 0.12
- north_vel: float32 [16, 128, 4096], P(None, 'lat', 'lon'), may hold values from -0.12 to 0.12
- vertical_vel: float32 [16, 128, 4096], P(None, 'lat', 'lon'), may hold values from -0.12 to 0.12
- diffusivity: float32 [16, 128, 4096], P(None, 'lat', 'lon'), may hold values from 0.01 to 0.04
- sea_mask: int32 [16, 128, 4096], P(None, 'lat', 'lon'), may hold values 0 or 1
- reaction_rate: float32 [3, 16], replicated, may hold values from 0.05 to 0.5
- fold_partner: int32 [4096], P('lon'), may hold values from 0 to 4095, as said below
Outputs:
- source_grad: float32 [3, 16, 128, 4096], P(None, None, 'lat', 'lon')
- grad_norm: float32 [], replicated
The draws below stay inside these ranges and needn't reach their ends.
Inputs may be any that keep to these rules, and one draw needn't show every extreme that they name: fold_partner[fold_partner[i]] = i; column i meets column (s - i) mod 4096 across the fold, for one s of each draw.
All inputs are finite; a program needn't handle non-finite values. No bound on the sum of `sea_mask` on one device may be relied on, other than what follows from the above.
Results may differ from the reference program's by a relative error of at most 0.00002.
Values sent between devices are 32-bit elements; how exact they have to be, the bound alone decides.
No kernel may reach another device: no remote copies, remote signals or barrier semaphores. Data moves between devices by JAX's collectives and lax.ppermute only.
A program may use at most 64 MiB of HBM per device.

```python
import math
import jax
import jax.numpy as jnp
from jax import lax

LEV = 16
NTR = 3
STEPS = 4
NX = 4096
NY = 128


def draw_target(key, part):
    lon_pos = jnp.arange(NX, dtype=jnp.float32) / NX
    lat_pos = jnp.arange(NY, dtype=jnp.float32) / NY
    scale = 0.5 * jnp.exp(jnp.log(3.0) * (lat_pos[:, None] + lon_pos[None, :]))
    base = jnp.clip(jax.random.normal(key, (NTR, LEV, NY, NX), jnp.float32), -6.0, 6.0)
    return base * scale


def draw_fold_partner(key, part):
    offset = jax.random.randint(key, (), 0, NX, dtype=jnp.int32)
    return (offset - jnp.arange(NX, dtype=jnp.int32)) % NX


def plant(array, rng, least, largest):
    longest = array.shape.index(max(array.shape))
    spots = []
    for shift in (0, 1):
        where = [jax.random.randint(jax.random.fold_in(rng, axis), (), 0, length) for axis, length in enumerate(array.shape)]
        where[longest] = (where[longest] + shift) % array.shape[longest]
        spots.append(tuple(where))
    return array.at[spots[0]].set(least).at[spots[1]].set(largest)


def shard_levels(stream_key, dims, shards, least, top_value):
    def one(axis_at, parts):
        steps = jax.random.uniform(jax.random.fold_in(jax.random.fold_in(stream_key, 6), axis_at), (parts,), jnp.float32, least / len(shards), top_value / len(shards))
        return jnp.repeat(jnp.exp(steps), dims[axis_at] // parts).reshape((-1,) + (1,) * (len(dims) - axis_at - 1))

    gain = one(*shards[0])
    for cut in shards[1:]:
        gain = gain * one(*cut)
    return gain


def bell_draw(key, extent, width, reach, pieces=(), kind=jnp.bfloat16):
    loudness = shard_levels(key, extent, pieces, -0.22, 0.18) if pieces else 1.0
    array = jax.random.normal(key, extent, jnp.float32) * width * loudness
    return jnp.minimum(jnp.maximum(array, -reach), reach).astype(kind)


def setup_inputs(seed: int = 0) -> dict:
    key_of = jax.random.split(jax.random.key(seed), 11)
    tracer_start = bell_draw(key_of[0], (NTR, LEV, NY, NX), 1.0, 6.0, ((2, 8), (3, 32)), jnp.float32)
    source = bell_draw(key_of[1], (NTR, LEV, NY, NX), 0.5, 3.0, ((2, 8), (3, 32)), jnp.float32)
    target = draw_target(jax.random.fold_in(key_of[10], 71), 0)
    east_vel = jnp.clip(jax.random.uniform(key_of[3], (LEV, NY, NX), jnp.float32, -0.12, 0.12) * shard_levels(key_of[3], (LEV, NY, NX), ((1, 8), (2, 32)), -0.4, 0.0), -0.12, 0.12)
    north_vel = jnp.clip(jax.random.uniform(key_of[4], (LEV, NY, NX), jnp.float32, -0.12, 0.12) * shard_levels(key_of[4], (LEV, NY, NX), ((1, 8), (2, 32)), -0.4, 0.0), -0.12, 0.12)
    vertical_vel = jnp.clip(jax.random.uniform(key_of[5], (LEV, NY, NX), jnp.float32, -0.12, 0.12) * shard_levels(key_of[5], (LEV, NY, NX), ((1, 8), (2, 32)), -0.4, 0.0), -0.12, 0.12)
    diffusivity = jnp.clip(0.01 + 0.03 * jax.random.uniform(key_of[6], (LEV, NY, NX), jnp.float32) ** shard_levels(key_of[6], (LEV, NY, NX), ((1, 8), (2, 32)), -0.2, 0.2), 0.01, 0.04)
    sea_mask = plant((jax.random.randint(key_of[7], (LEV, NY, NX), 0, 5) < 4).astype(jnp.int32), jax.random.fold_in(key_of[7], 1), 0, 1)
    reaction_rate = jnp.clip(jnp.exp(jax.random.uniform(key_of[8], (NTR, LEV), jnp.float32, math.log(0.05), math.log(0.5))), 0.05, 0.5)
    fold_partner = draw_fold_partner(jax.random.fold_in(key_of[10], 71), 0)
    return dict(tracer_start=tracer_start, source=source, target=target, east_vel=east_vel, north_vel=north_vel, vertical_vel=vertical_vel, diffusivity=diffusivity, sea_mask=sea_mask, reaction_rate=reaction_rate, fold_partner=fold_partner)


def upwind_pair(velocity, mixing, face_sea):
    flow_rate = velocity * face_sea
    mixing_part = mixing * face_sea
    return (jnp.maximum(flow_rate, 0.0) + mixing_part, jnp.minimum(flow_rate, 0.0) - mixing_part)

def next_row(values, axis):
    upper = lax.slice_in_dim(values, 1, values.shape[axis], axis=axis)
    empty = jnp.zeros_like(lax.slice_in_dim(values, 0, 1, axis=axis))
    return jnp.concatenate([upper, empty], axis)

def prev_row(values, axis):
    lower = lax.slice_in_dim(values, 0, values.shape[axis] - 1, axis=axis)
    empty = jnp.zeros_like(lax.slice_in_dim(values, 0, 1, axis=axis))
    return jnp.concatenate([empty, lower], axis)

def reference(tracer_start, source, target, east_vel, north_vel, vertical_vel, diffusivity, sea_mask, reaction_rate, fold_partner):
    ocean = sea_mask.astype(jnp.float32)
    east_own, east_next = upwind_pair(east_vel, 0.5 * (diffusivity + jnp.roll(diffusivity, -1, 2)), ocean * jnp.roll(ocean, -1, 2))
    north_own, north_next = upwind_pair(north_vel, 0.5 * (diffusivity + next_row(diffusivity, 1)), ocean * next_row(ocean, 1))
    up_own, up_next = upwind_pair(vertical_vel, 0.5 * (diffusivity + next_row(diffusivity, 0)), ocean * next_row(ocean, 0))
    top_vel = north_vel[:, -1, :]
    top_mix = diffusivity[:, -1, :]
    top_sea = ocean[:, -1, :]
    fold_own, fold_next = upwind_pair(0.5 * (top_vel - jnp.take(top_vel, fold_partner, axis=1)), 0.5 * (top_mix + jnp.take(top_mix, fold_partner, axis=1)), top_sea * jnp.take(top_sea, fold_partner, axis=1))

    def one_tracer(inputs):
        start, forcing, observed, rates = inputs
        decay_rate = rates[:, None, None]

        def divergence(quantity):
            east_flux = east_own * quantity + east_next * jnp.roll(quantity, -1, 2)
            north_flux = north_own * quantity + north_next * next_row(quantity, 1)
            top_row = quantity[:, -1, :]
            fold_flux = fold_own * top_row + fold_next * jnp.take(top_row, fold_partner, axis=1)
            north_flux = north_flux.at[:, -1, :].add(fold_flux)
            up_flux = up_own * quantity + up_next * next_row(quantity, 0)
            return east_flux - jnp.roll(east_flux, 1, 2) + (north_flux - prev_row(north_flux, 1)) + (up_flux - prev_row(up_flux, 0))

        def advance(quantity):
            uptake = decay_rate * quantity / jnp.sqrt(1.0 + quantity * quantity)
            return ocean * (quantity - divergence(quantity) - uptake + forcing)
        states = [start]
        for repeat in range(STEPS):
            states.append(advance(states[-1]))
        adjoint = ocean * (states[-1] - observed)
        gradient = ocean * adjoint
        for backward in range(STEPS - 1, 0, -1):
            unused, pull = jax.vjp(advance, states[backward])
            adjoint = pull(adjoint)[0]
            gradient = gradient + ocean * adjoint
        return gradient
    source_grad = lax.map(one_tracer, (tracer_start, source, target, reaction_rate))
    grad_norm = jnp.sqrt(jnp.sum(source_grad * source_grad))
    return (source_grad, grad_norm)
```

```python
import jax
import jax.numpy as jnp
from jax import lax
from jax.sharding import PartitionSpec as P

STEPS = 4


def with_halo(block, sides, width, periodic):
    for axis, dim in sides:
        count = lax.axis_size(axis)
        forward = [(i, i + 1) for i in range(count - 1)]
        if periodic:
            forward.append((count - 1, 0))
        backward = [(target, source) for source, target in forward]
        low = lax.ppermute(
            lax.slice_in_dim(block, block.shape[dim] - width, None, axis=dim), axis, forward
        )
        high = lax.ppermute(lax.slice_in_dim(block, 0, width, axis=dim), axis, backward)
        block = jnp.concatenate([low, block, high], axis=dim)
    return block


def fold_row(row, fold_partner):
    count = lax.axis_size("lon")
    width = row.shape[-1]
    here = lax.axis_index("lon")
    whole = width * count
    offset = (fold_partner[0] + width * here) % whole
    turns = offset // width
    shift = offset % width
    flipped = row[..., ::-1]
    first = lax.ppermute(flipped, "lon", [((-d) % count, d) for d in range(count)])
    second = lax.ppermute(flipped, "lon", [((-d - 1) % count, d) for d in range(count)])
    pair = jnp.concatenate([first, second], axis=-1)
    step = 1
    while step < count:
        moved = lax.ppermute(pair, "lon", [(d, (d + step) % count) for d in range(count)])
        pair = jnp.where((turns // step) % 2 == 1, moved, pair)
        step *= 2
    return lax.dynamic_slice_in_dim(pair, width - 1 - shift, width, axis=pair.ndim - 1)


def tree_sum(value, axis):
    count = lax.axis_size(axis)
    if count & (count - 1):
        return lax.psum(value, axis)
    step = 1
    while step < count:
        value = value + lax.ppermute(value, axis, [(d, d ^ step) for d in range(count)])
        step *= 2
    return value


def upwind_pair(velocity, mixing, face_sea):
    flow_rate = velocity * face_sea
    mixing_part = mixing * face_sea
    return (jnp.maximum(flow_rate, 0.0) + mixing_part, jnp.minimum(flow_rate, 0.0) - mixing_part)


def on_device(
    tracer_start,
    source,
    target,
    east_vel,
    north_vel,
    vertical_vel,
    diffusivity,
    sea_mask,
    reaction_rate,
    fold_partner,
):
    ocean = sea_mask.astype(jnp.float32)
    statics = jnp.stack([east_vel, north_vel, diffusivity, ocean])
    wide_static = with_halo(statics, (("lon", 3),), 1, True)
    tall_static = with_halo(statics, (("lat", 2),), 1, False)
    west_cell = wide_static[..., :-1]
    east_cell = wide_static[..., 1:]
    east_own, east_next = upwind_pair(
        west_cell[0], 0.5 * (west_cell[2] + east_cell[2]), west_cell[3] * east_cell[3]
    )
    below_row = tall_static[:, :, :-1, :]
    above_row = tall_static[:, :, 1:, :]
    north_own, north_next = upwind_pair(
        below_row[1], 0.5 * (below_row[2] + above_row[2]), below_row[3] * above_row[3]
    )
    up_own, up_next = upwind_pair(
        vertical_vel[:-1], 0.5 * (diffusivity[:-1] + diffusivity[1:]), ocean[:-1] * ocean[1:]
    )
    top_static = jnp.stack([north_vel[:, -1, :], diffusivity[:, -1, :], ocean[:, -1, :]])
    across = fold_row(top_static, fold_partner)
    north_top = (lax.axis_index("lat") == lax.axis_size("lat") - 1).astype(jnp.float32)
    fold_own, fold_next = upwind_pair(
        0.5 * (top_static[0] - across[0]),
        0.5 * (top_static[1] + across[1]),
        top_static[2] * across[2] * north_top,
    )
    decay_rate = reaction_rate[:, :, None, None]

    def neighbours(quantity):
        east_west = with_halo(quantity, (("lon", 3),), 1, True)
        south_north = with_halo(quantity, (("lat", 2),), 1, False)
        top_row = quantity[:, :, -1, :]
        partner_row = fold_row(top_row, fold_partner)
        return (east_west, south_north, partner_row)

    kept_states = [tracer_start]
    for repeat in range(STEPS):
        advance_quantity = kept_states[-1]
        uptake = decay_rate * advance_quantity / jnp.sqrt(1.0 + advance_quantity * advance_quantity)
        divergence_east_west, divergence_south_north, divergence_partner_row = neighbours(
            advance_quantity
        )
        east_flux = (
            east_own * divergence_east_west[..., :-1] + east_next * divergence_east_west[..., 1:]
        )
        north_flux = (
            north_own * divergence_south_north[:, :, :-1, :]
            + north_next * divergence_south_north[:, :, 1:, :]
        )
        divergence_top_row = advance_quantity[:, :, -1, :]
        fold_flux = fold_own * divergence_top_row + fold_next * divergence_partner_row
        north_flux = north_flux.at[:, :, -1, :].add(fold_flux)
        up_flux = up_own * advance_quantity[:, :-1] + up_next * advance_quantity[:, 1:]
        zero_level = jnp.zeros_like(advance_quantity[:, :1])
        vertical_part = jnp.concatenate([up_flux, zero_level], 1) - jnp.concatenate(
            [zero_level, up_flux], 1
        )
        kept_states.append(
            ocean
            * (
                advance_quantity
                - (
                    east_flux[..., 1:]
                    - east_flux[..., :-1]
                    + (north_flux[:, :, 1:, :] - north_flux[:, :, :-1, :])
                    + vertical_part
                )
                - uptake
                + source
            )
        )
    last_state = kept_states[-1]
    adjoint = ocean * (last_state - target)
    source_grad = ocean * adjoint
    for backward in range(STEPS - 1, 0, -1):
        current = kept_states[backward]
        weight = ocean * adjoint
        transposed_east_west, transposed_south_north, transposed_partner_row = neighbours(weight)
        east_diff = transposed_east_west[..., :-1] - transposed_east_west[..., 1:]
        north_diff = transposed_south_north[:, :, :-1, :] - transposed_south_north[:, :, 1:, :]
        up_diff = weight[:, :-1] - weight[:, 1:]
        result = east_own[..., 1:] * east_diff[..., 1:] + east_next[..., :-1] * east_diff[..., :-1]
        result = result + (
            north_own[:, 1:, :] * north_diff[:, :, 1:, :]
            + north_next[:, :-1, :] * north_diff[:, :, :-1, :]
        )
        result = result.at[:, :, -1, :].add(
            fold_own * (weight[:, :, -1, :] - transposed_partner_row)
        )
        transposed_zero_level = jnp.zeros_like(weight[:, :1])
        result = result + (
            jnp.concatenate([up_own * up_diff, transposed_zero_level], 1)
            + jnp.concatenate([transposed_zero_level, up_next * up_diff], 1)
        )
        spread = 1.0 + current * current
        adjoint = weight - result - decay_rate / (spread * jnp.sqrt(spread)) * weight
        source_grad = source_grad + ocean * adjoint
    squares = tree_sum(tree_sum(jnp.sum(source_grad * source_grad), "lon"), "lat")
    return (source_grad, jnp.sqrt(squares))


def solution(mesh):
    return jax.shard_map(
        on_device,
        mesh=mesh,
        in_specs=(
            P(None, None, "lat", "lon"),
            P(None, None, "lat", "lon"),
            P(None, None, "lat", "lon"),
            P(None, "lat", "lon"),
            P(None, "lat", "lon"),
            P(None, "lat", "lon"),
            P(None, "lat", "lon"),
            P(None, "lat", "lon"),
            P(),
            P("lon"),
        ),
        out_specs=(P(None, None, "lat", "lon"), P()),
        check_vma=False,
    )
```

```python
import jax
import jax.numpy as jnp
from jax import lax
from jax.sharding import PartitionSpec as P

STEPS = 4


def with_halo(block, sides, width, periodic):
    for axis, dim in sides:
        count = lax.axis_size(axis)
        forward = [(i, i + 1) for i in range(count - 1)]
        if periodic:
            forward.append((count - 1, 0))
        backward = [(target, source) for source, target in forward]
        low = lax.ppermute(
            lax.slice_in_dim(block, block.shape[dim] - width, None, axis=dim), axis, forward
        )
        high = lax.ppermute(lax.slice_in_dim(block, 0, width, axis=dim), axis, backward)
        block = jnp.concatenate([low, block, high], axis=dim)
    return block


def fold_row(row, fold_partner, radix=8):
    count = lax.axis_size("lon")
    width = row.shape[-1]
    here = lax.axis_index("lon")
    offset = (fold_partner[0] + width * here) % (width * count)
    turns = offset // width
    shift = offset % width
    radix = min(radix, count)
    low = turns % radix
    high = turns // radix
    flipped = row[..., ::-1]
    mirrored = [
        lax.ppermute(flipped, "lon", [((k - d) % count, d) for d in range(count)])
        for k in range(-1, radix)
    ]
    pair = jnp.concatenate(
        [lax.select_n(low, *mirrored[1:]), lax.select_n(low, *mirrored[:-1])], axis=-1
    )
    moved = [pair] + [
        lax.ppermute(pair, "lon", [(d, (d + radix * b) % count) for d in range(count)])
        for b in range(1, -(-count // radix))
    ]
    if len(moved) > 1:
        pair = lax.select_n(high, *moved)
    return lax.dynamic_slice_in_dim(pair, width - 1 - shift, width, axis=pair.ndim - 1)


def group_sum(value, axis, stride, radix):
    here = lax.axis_index(axis)
    digit = (here // stride) % radix
    count = lax.axis_size(axis)
    got = [value]
    for o in range(1, radix):
        pairs = []
        for d in range(count):
            g = (d // stride) % radix
            pairs.append((d + ((g + o) % radix - g) * stride, d))
        got.append(lax.ppermute(value, axis, pairs))
    total = None
    for j in range(radix):
        part = lax.select_n((j - digit) % radix, *got)
        total = part if total is None else total + part
    return total


def tree_sum(value, axis):
    count = lax.axis_size(axis)
    stride = 1
    while stride < count:
        radix = 8 if (count // stride) % 8 == 0 and count // stride != 16 else 4
        if (count // stride) % radix:
            radix = count // stride
        value = group_sum(value, axis, stride, radix)
        stride *= radix
    return value


def upwind_pair(velocity, mixing, face_sea):
    flow_rate = velocity * face_sea
    mixing_part = mixing * face_sea
    return (jnp.maximum(flow_rate, 0.0) + mixing_part, jnp.minimum(flow_rate, 0.0) - mixing_part)


def on_device(
    tracer_start,
    source,
    target,
    east_vel,
    north_vel,
    vertical_vel,
    diffusivity,
    sea_mask,
    reaction_rate,
    fold_partner,
):
    ocean = sea_mask.astype(jnp.float32)
    statics = jnp.stack([east_vel, north_vel, diffusivity, ocean])
    wide_static = with_halo(statics, (("lon", 3),), 1, True)
    tall_static = with_halo(statics, (("lat", 2),), 1, False)
    west_cell = wide_static[..., :-1]
    east_cell = wide_static[..., 1:]
    east_own, east_next = upwind_pair(
        west_cell[0], 0.5 * (west_cell[2] + east_cell[2]), west_cell[3] * east_cell[3]
    )
    below_row = tall_static[:, :, :-1, :]
    above_row = tall_static[:, :, 1:, :]
    north_own, north_next = upwind_pair(
        below_row[1], 0.5 * (below_row[2] + above_row[2]), below_row[3] * above_row[3]
    )
    up_own, up_next = upwind_pair(
        vertical_vel[:-1], 0.5 * (diffusivity[:-1] + diffusivity[1:]), ocean[:-1] * ocean[1:]
    )
    top_static = jnp.stack([north_vel[:, -1, :], diffusivity[:, -1, :], ocean[:, -1, :]])
    across = fold_row(top_static, fold_partner)
    north_top = (lax.axis_index("lat") == lax.axis_size("lat") - 1).astype(jnp.float32)
    fold_own, fold_next = upwind_pair(
        0.5 * (top_static[0] - across[0]),
        0.5 * (top_static[1] + across[1]),
        top_static[2] * across[2] * north_top,
    )
    decay_rate = reaction_rate[:, :, None, None]

    def neighbours(quantity):
        east_west = with_halo(quantity, (("lon", 3),), 1, True)
        south_north = with_halo(quantity, (("lat", 2),), 1, False)
        top_row = quantity[:, :, -1, :]
        partner_row = fold_row(top_row, fold_partner)
        return (east_west, south_north, partner_row)

    kept_states = [tracer_start]
    for repeat in range(STEPS):
        advance_quantity = kept_states[-1]
        uptake = decay_rate * advance_quantity / jnp.sqrt(1.0 + advance_quantity * advance_quantity)
        divergence_east_west, divergence_south_north, divergence_partner_row = neighbours(
            advance_quantity
        )
        east_flux = (
            east_own * divergence_east_west[..., :-1] + east_next * divergence_east_west[..., 1:]
        )
        north_flux = (
            north_own * divergence_south_north[:, :, :-1, :]
            + north_next * divergence_south_north[:, :, 1:, :]
        )
        divergence_top_row = advance_quantity[:, :, -1, :]
        fold_flux = fold_own * divergence_top_row + fold_next * divergence_partner_row
        north_flux = north_flux.at[:, :, -1, :].add(fold_flux)
        up_flux = up_own * advance_quantity[:, :-1] + up_next * advance_quantity[:, 1:]
        zero_level = jnp.zeros_like(advance_quantity[:, :1])
        vertical_part = jnp.concatenate([up_flux, zero_level], 1) - jnp.concatenate(
            [zero_level, up_flux], 1
        )
        kept_states.append(
            ocean
            * (
                advance_quantity
                - (
                    east_flux[..., 1:]
                    - east_flux[..., :-1]
                    + (north_flux[:, :, 1:, :] - north_flux[:, :, :-1, :])
                    + vertical_part
                )
                - uptake
                + source
            )
        )
    last_state = kept_states[-1]
    adjoint = ocean * (last_state - target)
    source_grad = ocean * adjoint
    for backward in range(STEPS - 1, 0, -1):
        current = kept_states[backward]
        weight = ocean * adjoint
        transposed_east_west, transposed_south_north, transposed_partner_row = neighbours(weight)
        east_diff = transposed_east_west[..., :-1] - transposed_east_west[..., 1:]
        north_diff = transposed_south_north[:, :, :-1, :] - transposed_south_north[:, :, 1:, :]
        up_diff = weight[:, :-1] - weight[:, 1:]
        result = east_own[..., 1:] * east_diff[..., 1:] + east_next[..., :-1] * east_diff[..., :-1]
        result = result + (
            north_own[:, 1:, :] * north_diff[:, :, 1:, :]
            + north_next[:, :-1, :] * north_diff[:, :, :-1, :]
        )
        result = result.at[:, :, -1, :].add(
            fold_own * (weight[:, :, -1, :] - transposed_partner_row)
        )
        transposed_zero_level = jnp.zeros_like(weight[:, :1])
        result = result + (
            jnp.concatenate([up_own * up_diff, transposed_zero_level], 1)
            + jnp.concatenate([transposed_zero_level, up_next * up_diff], 1)
        )
        spread = 1.0 + current * current
        adjoint = weight - result - decay_rate / (spread * jnp.sqrt(spread)) * weight
        source_grad = source_grad + ocean * adjoint
    squares = tree_sum(tree_sum(jnp.sum(source_grad * source_grad), "lon"), "lat")
    return (source_grad, jnp.sqrt(squares))


def solution(mesh):
    return jax.shard_map(
        on_device,
        mesh=mesh,
        in_specs=(
            P(None, None, "lat", "lon"),
            P(None, None, "lat", "lon"),
            P(None, None, "lat", "lon"),
            P(None, "lat", "lon"),
            P(None, "lat", "lon"),
            P(None, "lat", "lon"),
            P(None, "lat", "lon"),
            P(None, "lat", "lon"),
            P(),
            P("lon"),
        ),
        out_specs=(P(None, None, "lat", "lon"), P()),
        check_vma=False,
    )
```

```python
import jax
import jax.numpy as jnp
from jax import lax
from jax.sharding import PartitionSpec as P

STEPS = 4


def with_halo(block, sides, width, periodic):
    for axis, dim in sides:
        count = lax.axis_size(axis)
        forward = [(i, i + 1) for i in range(count - 1)]
        if periodic:
            forward.append((count - 1, 0))
        backward = [(target, source) for source, target in forward]
        low = lax.ppermute(
            lax.slice_in_dim(block, block.shape[dim] - width, None, axis=dim), axis, forward
        )
        high = lax.ppermute(lax.slice_in_dim(block, 0, width, axis=dim), axis, backward)
        block = jnp.concatenate([low, block, high], axis=dim)
    return block


def fold_row(row, fold_partner):
    count = lax.axis_size("lon")
    width = row.shape[-1]
    here = lax.axis_index("lon")
    offset = (fold_partner[0] + width * here) % (width * count)
    turns = offset // width
    shift = offset % width
    flipped = row[..., ::-1]
    slots = jnp.arange(count).reshape((count,) + (1,) * row.ndim)
    wanted = (slots == (turns - here) % count) | (slots == (turns - here - 1) % count)
    sent = jnp.where(wanted, flipped[None], 0.0)
    got = lax.all_to_all(sent, "lon", 0, 0)
    first = lax.dynamic_index_in_dim(got, (turns - here) % count, 0, keepdims=False)
    second = lax.dynamic_index_in_dim(got, (turns - here - 1) % count, 0, keepdims=False)
    pair = jnp.concatenate([first, second], axis=-1)
    return lax.dynamic_slice_in_dim(pair, width - 1 - shift, width, axis=pair.ndim - 1)


def tree_sum(value, axes):
    count = 1
    for axis in axes:
        count *= lax.axis_size(axis)
    got = lax.all_to_all(jnp.broadcast_to(value, (count,)), axes, 0, 0)
    total = got[0]
    for j in range(1, count):
        total = total + got[j]
    return total


def upwind_pair(velocity, mixing, face_sea):
    flow_rate = velocity * face_sea
    mixing_part = mixing * face_sea
    return (jnp.maximum(flow_rate, 0.0) + mixing_part, jnp.minimum(flow_rate, 0.0) - mixing_part)


def on_device(
    tracer_start,
    source,
    target,
    east_vel,
    north_vel,
    vertical_vel,
    diffusivity,
    sea_mask,
    reaction_rate,
    fold_partner,
):
    ocean = sea_mask.astype(jnp.float32)
    statics = jnp.stack([east_vel, north_vel, diffusivity, ocean])
    wide_static = with_halo(statics, (("lon", 3),), 1, True)
    tall_static = with_halo(statics, (("lat", 2),), 1, False)
    west_cell = wide_static[..., :-1]
    east_cell = wide_static[..., 1:]
    east_own, east_next = upwind_pair(
        west_cell[0], 0.5 * (west_cell[2] + east_cell[2]), west_cell[3] * east_cell[3]
    )
    below_row = tall_static[:, :, :-1, :]
    above_row = tall_static[:, :, 1:, :]
    north_own, north_next = upwind_pair(
        below_row[1], 0.5 * (below_row[2] + above_row[2]), below_row[3] * above_row[3]
    )
    up_own, up_next = upwind_pair(
        vertical_vel[:-1], 0.5 * (diffusivity[:-1] + diffusivity[1:]), ocean[:-1] * ocean[1:]
    )
    top_static = jnp.stack([north_vel[:, -1, :], diffusivity[:, -1, :], ocean[:, -1, :]])
    across = fold_row(top_static, fold_partner)
    north_top = (lax.axis_index("lat") == lax.axis_size("lat") - 1).astype(jnp.float32)
    fold_own, fold_next = upwind_pair(
        0.5 * (top_static[0] - across[0]),
        0.5 * (top_static[1] + across[1]),
        top_static[2] * across[2] * north_top,
    )
    decay_rate = reaction_rate[:, :, None, None]

    def neighbours(quantity):
        east_west = with_halo(quantity, (("lon", 3),), 1, True)
        south_north = with_halo(quantity, (("lat", 2),), 1, False)
        top_row = quantity[:, :, -1, :]
        partner_row = fold_row(top_row, fold_partner)
        return (east_west, south_north, partner_row)

    kept_states = [tracer_start]
    for repeat in range(STEPS):
        advance_quantity = kept_states[-1]
        uptake = decay_rate * advance_quantity / jnp.sqrt(1.0 + advance_quantity * advance_quantity)
        divergence_east_west, divergence_south_north, divergence_partner_row = neighbours(
            advance_quantity
        )
        east_flux = (
            east_own * divergence_east_west[..., :-1] + east_next * divergence_east_west[..., 1:]
        )
        north_flux = (
            north_own * divergence_south_north[:, :, :-1, :]
            + north_next * divergence_south_north[:, :, 1:, :]
        )
        divergence_top_row = advance_quantity[:, :, -1, :]
        fold_flux = fold_own * divergence_top_row + fold_next * divergence_partner_row
        north_flux = north_flux.at[:, :, -1, :].add(fold_flux)
        up_flux = up_own * advance_quantity[:, :-1] + up_next * advance_quantity[:, 1:]
        zero_level = jnp.zeros_like(advance_quantity[:, :1])
        vertical_part = jnp.concatenate([up_flux, zero_level], 1) - jnp.concatenate(
            [zero_level, up_flux], 1
        )
        kept_states.append(
            ocean
            * (
                advance_quantity
                - (
                    east_flux[..., 1:]
                    - east_flux[..., :-1]
                    + (north_flux[:, :, 1:, :] - north_flux[:, :, :-1, :])
                    + vertical_part
                )
                - uptake
                + source
            )
        )
    last_state = kept_states[-1]
    adjoint = ocean * (last_state - target)
    source_grad = ocean * adjoint
    for backward in range(STEPS - 1, 0, -1):
        current = kept_states[backward]
        weight = ocean * adjoint
        transposed_east_west, transposed_south_north, transposed_partner_row = neighbours(weight)
        east_diff = transposed_east_west[..., :-1] - transposed_east_west[..., 1:]
        north_diff = transposed_south_north[:, :, :-1, :] - transposed_south_north[:, :, 1:, :]
        up_diff = weight[:, :-1] - weight[:, 1:]
        result = east_own[..., 1:] * east_diff[..., 1:] + east_next[..., :-1] * east_diff[..., :-1]
        result = result + (
            north_own[:, 1:, :] * north_diff[:, :, 1:, :]
            + north_next[:, :-1, :] * north_diff[:, :, :-1, :]
        )
        result = result.at[:, :, -1, :].add(
            fold_own * (weight[:, :, -1, :] - transposed_partner_row)
        )
        transposed_zero_level = jnp.zeros_like(weight[:, :1])
        result = result + (
            jnp.concatenate([up_own * up_diff, transposed_zero_level], 1)
            + jnp.concatenate([transposed_zero_level, up_next * up_diff], 1)
        )
        spread = 1.0 + current * current
        adjoint = weight - result - decay_rate / (spread * jnp.sqrt(spread)) * weight
        source_grad = source_grad + ocean * adjoint
    squares = tree_sum(jnp.sum(source_grad * source_grad), ("lon", "lat"))
    return (source_grad, jnp.sqrt(squares))


def solution(mesh):
    return jax.shard_map(
        on_device,
        mesh=mesh,
        in_specs=(
            P(None, None, "lat", "lon"),
            P(None, None, "lat", "lon"),
            P(None, None, "lat", "lon"),
            P(None, "lat", "lon"),
            P(None, "lat", "lon"),
            P(None, "lat", "lon"),
            P(None, "lat", "lon"),
            P(None, "lat", "lon"),
            P(),
            P("lon"),
        ),
        out_specs=(P(None, None, "lat", "lon"), P()),
        check_vma=False,
    )
```

```python
import jax
import jax.numpy as jnp
from jax import lax
from jax.sharding import PartitionSpec as P

STEPS = 4


def with_halo(block, sides, width, periodic):
    for axis, dim in sides:
        count = lax.axis_size(axis)
        forward = [(i, i + 1) for i in range(count - 1)]
        if periodic:
            forward.append((count - 1, 0))
        backward = [(target, source) for source, target in forward]
        low = lax.ppermute(
            lax.slice_in_dim(block, block.shape[dim] - width, None, axis=dim), axis, forward
        )
        high = lax.ppermute(lax.slice_in_dim(block, 0, width, axis=dim), axis, backward)
        block = jnp.concatenate([low, block, high], axis=dim)
    return block


def fold_row(row, fold_partner):
    count = lax.axis_size("lon")
    width = row.shape[-1]
    here = lax.axis_index("lon")
    offset = (fold_partner[0] + width * here) % (width * count)
    turns = offset // width
    shift = offset % width
    flipped = row[..., ::-1]
    slots = jnp.arange(count).reshape((count,) + (1,) * row.ndim)
    wanted = (slots == (turns - here) % count) | (slots == (turns - here - 1) % count)
    sent = jnp.where(wanted, flipped[None], 0.0)
    got = lax.all_to_all(sent, "lon", 0, 0)
    first = lax.dynamic_index_in_dim(got, (turns - here) % count, 0, keepdims=False)
    second = lax.dynamic_index_in_dim(got, (turns - here - 1) % count, 0, keepdims=False)
    pair = jnp.concatenate([first, second], axis=-1)
    return lax.dynamic_slice_in_dim(pair, width - 1 - shift, width, axis=pair.ndim - 1)


def tree_sum(value, axes):
    count = 1
    for axis in axes:
        count *= lax.axis_size(axis)
    got = lax.all_to_all(jnp.broadcast_to(value, (count,)), axes, 0, 0)
    return jnp.sum(got)


def upwind_pair(velocity, mixing, face_sea):
    flow_rate = velocity * face_sea
    mixing_part = mixing * face_sea
    return (jnp.maximum(flow_rate, 0.0) + mixing_part, jnp.minimum(flow_rate, 0.0) - mixing_part)


def on_device(
    tracer_start,
    source,
    target,
    east_vel,
    north_vel,
    vertical_vel,
    diffusivity,
    sea_mask,
    reaction_rate,
    fold_partner,
):
    ocean = sea_mask.astype(jnp.float32)
    statics = jnp.stack([east_vel, north_vel, diffusivity, ocean])
    wide_static = with_halo(statics, (("lon", 3),), 1, True)
    tall_static = with_halo(statics, (("lat", 2),), 1, False)
    west_cell = wide_static[..., :-1]
    east_cell = wide_static[..., 1:]
    east_own, east_next = upwind_pair(
        west_cell[0], 0.5 * (west_cell[2] + east_cell[2]), west_cell[3] * east_cell[3]
    )
    below_row = tall_static[:, :, :-1, :]
    above_row = tall_static[:, :, 1:, :]
    north_own, north_next = upwind_pair(
        below_row[1], 0.5 * (below_row[2] + above_row[2]), below_row[3] * above_row[3]
    )
    up_own, up_next = upwind_pair(
        vertical_vel[:-1], 0.5 * (diffusivity[:-1] + diffusivity[1:]), ocean[:-1] * ocean[1:]
    )
    top_static = jnp.stack([north_vel[:, -1, :], diffusivity[:, -1, :], ocean[:, -1, :]])
    across = fold_row(top_static, fold_partner)
    north_top = (lax.axis_index("lat") == lax.axis_size("lat") - 1).astype(jnp.float32)
    fold_own, fold_next = upwind_pair(
        0.5 * (top_static[0] - across[0]),
        0.5 * (top_static[1] + across[1]),
        top_static[2] * across[2] * north_top,
    )
    decay_rate = reaction_rate[:, :, None, None]

    def neighbours(quantity):
        east_west = with_halo(quantity, (("lon", 3),), 1, True)
        south_north = with_halo(quantity, (("lat", 2),), 1, False)
        top_row = quantity[:, :, -1, :]
        partner_row = fold_row(top_row, fold_partner)
        return (east_west, south_north, partner_row)

    kept_states = [tracer_start]
    for repeat in range(STEPS):
        advance_quantity = kept_states[-1]
        uptake = decay_rate * advance_quantity / jnp.sqrt(1.0 + advance_quantity * advance_quantity)
        divergence_east_west, divergence_south_north, divergence_partner_row = neighbours(
            advance_quantity
        )
        east_flux = (
            east_own * divergence_east_west[..., :-1] + east_next * divergence_east_west[..., 1:]
        )
        north_flux = (
            north_own * divergence_south_north[:, :, :-1, :]
            + north_next * divergence_south_north[:, :, 1:, :]
        )
        divergence_top_row = advance_quantity[:, :, -1, :]
        fold_flux = fold_own * divergence_top_row + fold_next * divergence_partner_row
        north_flux = north_flux.at[:, :, -1, :].add(fold_flux)
        up_flux = up_own * advance_quantity[:, :-1] + up_next * advance_quantity[:, 1:]
        zero_level = jnp.zeros_like(advance_quantity[:, :1])
        vertical_part = jnp.concatenate([up_flux, zero_level], 1) - jnp.concatenate(
            [zero_level, up_flux], 1
        )
        kept_states.append(
            ocean
            * (
                advance_quantity
                - (
                    east_flux[..., 1:]
                    - east_flux[..., :-1]
                    + (north_flux[:, :, 1:, :] - north_flux[:, :, :-1, :])
                    + vertical_part
                )
                - uptake
                + source
            )
        )
    last_state = kept_states[-1]
    adjoint = ocean * (last_state - target)
    source_grad = ocean * adjoint
    for backward in range(STEPS - 1, 0, -1):
        current = kept_states[backward]
        weight = ocean * adjoint
        transposed_east_west, transposed_south_north, transposed_partner_row = neighbours(weight)
        east_diff = transposed_east_west[..., :-1] - transposed_east_west[..., 1:]
        north_diff = transposed_south_north[:, :, :-1, :] - transposed_south_north[:, :, 1:, :]
        up_diff = weight[:, :-1] - weight[:, 1:]
        result = east_own[..., 1:] * east_diff[..., 1:] + east_next[..., :-1] * east_diff[..., :-1]
        result = result + (
            north_own[:, 1:, :] * north_diff[:, :, 1:, :]
            + north_next[:, :-1, :] * north_diff[:, :, :-1, :]
        )
        result = result.at[:, :, -1, :].add(
            fold_own * (weight[:, :, -1, :] - transposed_partner_row)
        )
        transposed_zero_level = jnp.zeros_like(weight[:, :1])
        result = result + (
            jnp.concatenate([up_own * up_diff, transposed_zero_level], 1)
            + jnp.concatenate([transposed_zero_level, up_next * up_diff], 1)
        )
        spread = 1.0 + current * current
        adjoint = weight - result - decay_rate / (spread * jnp.sqrt(spread)) * weight
        source_grad = source_grad + ocean * adjoint
    squares = tree_sum(jnp.sum(source_grad * source_grad), ("lon", "lat"))
    return (source_grad, jnp.sqrt(squares))


def solution(mesh):
    return jax.shard_map(
        on_device,
        mesh=mesh,
        in_specs=(
            P(None, None, "lat", "lon"),
            P(None, None, "lat", "lon"),
            P(None, None, "lat", "lon"),
            P(None, "lat", "lon"),
            P(None, "lat", "lon"),
            P(None, "lat", "lon"),
            P(None, "lat", "lon"),
            P(None, "lat", "lon"),
            P(),
            P("lon"),
        ),
        out_specs=(P(None, None, "lat", "lon"), P()),
        check_vma=False,
    )
```

```python
import jax
import jax.numpy as jnp
from jax import lax
from jax.sharding import PartitionSpec as P

STEPS = 4


def with_halo(block, sides, width, periodic):
    for axis, dim in sides:
        count = lax.axis_size(axis)
        forward = [(i, i + 1) for i in range(count - 1)]
        if periodic:
            forward.append((count - 1, 0))
        backward = [(target, source) for source, target in forward]
        low = lax.ppermute(
            lax.slice_in_dim(block, block.shape[dim] - width, None, axis=dim), axis, forward
        )
        high = lax.ppermute(lax.slice_in_dim(block, 0, width, axis=dim), axis, backward)
        block = jnp.concatenate([low, block, high], axis=dim)
    return block


def fold_row(row, fold_partner):
    count = lax.axis_size("lon")
    width = row.shape[-1]
    here = lax.axis_index("lon")
    offset = (fold_partner[0] + width * here) % (width * count)
    turns = offset // width
    shift = offset % width

    def branch(k):
        def move(flipped):
            first = lax.ppermute(flipped, "lon", [((k - d) % count, d) for d in range(count)])
            second = lax.ppermute(flipped, "lon", [((k - d - 1) % count, d) for d in range(count)])
            return jnp.concatenate([first, second], axis=-1)

        return move

    pair = lax.switch(turns, [branch(k) for k in range(count)], row[..., ::-1])
    return lax.dynamic_slice_in_dim(pair, width - 1 - shift, width, axis=pair.ndim - 1)


def tree_sum(value, axes):
    count = 1
    for axis in axes:
        count *= lax.axis_size(axis)
    got = lax.all_to_all(jnp.broadcast_to(value, (count,)), axes, 0, 0)
    return jnp.sum(got)


def upwind_pair(velocity, mixing, face_sea):
    flow_rate = velocity * face_sea
    mixing_part = mixing * face_sea
    return (jnp.maximum(flow_rate, 0.0) + mixing_part, jnp.minimum(flow_rate, 0.0) - mixing_part)


def on_device(
    tracer_start,
    source,
    target,
    east_vel,
    north_vel,
    vertical_vel,
    diffusivity,
    sea_mask,
    reaction_rate,
    fold_partner,
):
    ocean = sea_mask.astype(jnp.float32)
    statics = jnp.stack([east_vel, north_vel, diffusivity, ocean])
    wide_static = with_halo(statics, (("lon", 3),), 1, True)
    tall_static = with_halo(statics, (("lat", 2),), 1, False)
    west_cell = wide_static[..., :-1]
    east_cell = wide_static[..., 1:]
    east_own, east_next = upwind_pair(
        west_cell[0], 0.5 * (west_cell[2] + east_cell[2]), west_cell[3] * east_cell[3]
    )
    below_row = tall_static[:, :, :-1, :]
    above_row = tall_static[:, :, 1:, :]
    north_own, north_next = upwind_pair(
        below_row[1], 0.5 * (below_row[2] + above_row[2]), below_row[3] * above_row[3]
    )
    up_own, up_next = upwind_pair(
        vertical_vel[:-1], 0.5 * (diffusivity[:-1] + diffusivity[1:]), ocean[:-1] * ocean[1:]
    )
    top_static = jnp.stack([north_vel[:, -1, :], diffusivity[:, -1, :], ocean[:, -1, :]])
    across = fold_row(top_static, fold_partner)
    north_top = (lax.axis_index("lat") == lax.axis_size("lat") - 1).astype(jnp.float32)
    fold_own, fold_next = upwind_pair(
        0.5 * (top_static[0] - across[0]),
        0.5 * (top_static[1] + across[1]),
        top_static[2] * across[2] * north_top,
    )
    decay_rate = reaction_rate[:, :, None, None]

    def neighbours(quantity):
        east_west = with_halo(quantity, (("lon", 3),), 1, True)
        south_north = with_halo(quantity, (("lat", 2),), 1, False)
        top_row = quantity[:, :, -1, :]
        partner_row = fold_row(top_row, fold_partner)
        return (east_west, south_north, partner_row)

    kept_states = [tracer_start]
    for repeat in range(STEPS):
        advance_quantity = kept_states[-1]
        uptake = decay_rate * advance_quantity / jnp.sqrt(1.0 + advance_quantity * advance_quantity)
        divergence_east_west, divergence_south_north, divergence_partner_row = neighbours(
            advance_quantity
        )
        east_flux = (
            east_own * divergence_east_west[..., :-1] + east_next * divergence_east_west[..., 1:]
        )
        north_flux = (
            north_own * divergence_south_north[:, :, :-1, :]
            + north_next * divergence_south_north[:, :, 1:, :]
        )
        divergence_top_row = advance_quantity[:, :, -1, :]
        fold_flux = fold_own * divergence_top_row + fold_next * divergence_partner_row
        north_flux = north_flux.at[:, :, -1, :].add(fold_flux)
        up_flux = up_own * advance_quantity[:, :-1] + up_next * advance_quantity[:, 1:]
        zero_level = jnp.zeros_like(advance_quantity[:, :1])
        vertical_part = jnp.concatenate([up_flux, zero_level], 1) - jnp.concatenate(
            [zero_level, up_flux], 1
        )
        kept_states.append(
            ocean
            * (
                advance_quantity
                - (
                    east_flux[..., 1:]
                    - east_flux[..., :-1]
                    + (north_flux[:, :, 1:, :] - north_flux[:, :, :-1, :])
                    + vertical_part
                )
                - uptake
                + source
            )
        )
    last_state = kept_states[-1]
    adjoint = ocean * (last_state - target)
    source_grad = ocean * adjoint
    for backward in range(STEPS - 1, 0, -1):
        current = kept_states[backward]
        weight = ocean * adjoint
        transposed_east_west, transposed_south_north, transposed_partner_row = neighbours(weight)
        east_diff = transposed_east_west[..., :-1] - transposed_east_west[..., 1:]
        north_diff = transposed_south_north[:, :, :-1, :] - transposed_south_north[:, :, 1:, :]
        up_diff = weight[:, :-1] - weight[:, 1:]
        result = east_own[..., 1:] * east_diff[..., 1:] + east_next[..., :-1] * east_diff[..., :-1]
        result = result + (
            north_own[:, 1:, :] * north_diff[:, :, 1:, :]
            + north_next[:, :-1, :] * north_diff[:, :, :-1, :]
        )
        result = result.at[:, :, -1, :].add(
            fold_own * (weight[:, :, -1, :] - transposed_partner_row)
        )
        transposed_zero_level = jnp.zeros_like(weight[:, :1])
        result = result + (
            jnp.concatenate([up_own * up_diff, transposed_zero_level], 1)
            + jnp.concatenate([transposed_zero_level, up_next * up_diff], 1)
        )
        spread = 1.0 + current * current
        adjoint = weight - result - decay_rate / (spread * jnp.sqrt(spread)) * weight
        source_grad = source_grad + ocean * adjoint
    squares = tree_sum(jnp.sum(source_grad * source_grad), ("lon", "lat"))
    return (source_grad, jnp.sqrt(squares))


def solution(mesh):
    return jax.shard_map(
        on_device,
        mesh=mesh,
        in_specs=(
            P(None, None, "lat", "lon"),
            P(None, None, "lat", "lon"),
            P(None, None, "lat", "lon"),
            P(None, "lat", "lon"),
            P(None, "lat", "lon"),
            P(None, "lat", "lon"),
            P(None, "lat", "lon"),
            P(None, "lat", "lon"),
            P(),
            P("lon"),
        ),
        out_specs=(P(None, None, "lat", "lon"), P()),
        check_vma=False,
    )
```

```python
import jax
import jax.numpy as jnp
from jax import lax
from jax.sharding import PartitionSpec as P

STEPS = 4


def with_halo(block, sides, width, periodic):
    for axis, dim in sides:
        count = lax.axis_size(axis)
        forward = [(i, i + 1) for i in range(count - 1)]
        if periodic:
            forward.append((count - 1, 0))
        backward = [(target, source) for source, target in forward]
        low = lax.ppermute(
            lax.slice_in_dim(block, block.shape[dim] - width, None, axis=dim), axis, forward
        )
        high = lax.ppermute(lax.slice_in_dim(block, 0, width, axis=dim), axis, backward)
        block = jnp.concatenate([low, block, high], axis=dim)
    return block


def fold_row(row, fold_partner):
    count = lax.axis_size("lon")
    width = row.shape[-1]
    here = lax.axis_index("lon")
    offset = (fold_partner[0] + width * here) % (width * count)
    turns = offset // width
    shift = offset % width
    flipped = row[..., ::-1]
    slots = jnp.arange(count).reshape((count,) + (1,) * row.ndim)
    wanted = (slots == (turns - here) % count) | (slots == (turns - here - 1) % count)
    sent = jnp.where(wanted, flipped[None], 0.0)
    got = lax.all_to_all(sent, "lon", 0, 0)
    first = lax.dynamic_index_in_dim(got, (turns - here) % count, 0, keepdims=False)
    second = lax.dynamic_index_in_dim(got, (turns - here - 1) % count, 0, keepdims=False)
    pair = jnp.concatenate([first, second], axis=-1)
    return lax.dynamic_slice_in_dim(pair, width - 1 - shift, width, axis=pair.ndim - 1)


def tree_sum(value, axes):
    count = 1
    for axis in axes:
        count *= lax.axis_size(axis)
    got = lax.all_to_all(jnp.broadcast_to(value, (count,)), axes, 0, 0)
    return jnp.sum(got)


def upwind_pair(velocity, mixing, face_sea):
    flow_rate = velocity * face_sea
    mixing_part = mixing * face_sea
    return (jnp.maximum(flow_rate, 0.0) + mixing_part, jnp.minimum(flow_rate, 0.0) - mixing_part)


def on_device(
    tracer_start,
    source,
    target,
    east_vel,
    north_vel,
    vertical_vel,
    diffusivity,
    sea_mask,
    reaction_rate,
    fold_partner,
):
    ocean = sea_mask.astype(jnp.float32)
    statics = jnp.stack([east_vel, north_vel, diffusivity, ocean])
    wide_static = with_halo(statics, (("lon", 3),), 1, True)
    tall_static = with_halo(statics, (("lat", 2),), 1, False)
    west_cell = wide_static[..., :-1]
    east_cell = wide_static[..., 1:]
    east_own, east_next = upwind_pair(
        west_cell[0], 0.5 * (west_cell[2] + east_cell[2]), west_cell[3] * east_cell[3]
    )
    below_row = tall_static[:, :, :-1, :]
    above_row = tall_static[:, :, 1:, :]
    north_own, north_next = upwind_pair(
        below_row[1], 0.5 * (below_row[2] + above_row[2]), below_row[3] * above_row[3]
    )
    up_own, up_next = upwind_pair(
        vertical_vel[:-1], 0.5 * (diffusivity[:-1] + diffusivity[1:]), ocean[:-1] * ocean[1:]
    )
    top_static = jnp.stack([north_vel[:, -1, :], diffusivity[:, -1, :], ocean[:, -1, :]])
    across = fold_row(top_static, fold_partner)
    north_top = (lax.axis_index("lat") == lax.axis_size("lat") - 1).astype(jnp.float32)
    fold_own, fold_next = upwind_pair(
        0.5 * (top_static[0] - across[0]),
        0.5 * (top_static[1] + across[1]),
        top_static[2] * across[2] * north_top,
    )
    decay_rate = reaction_rate[:, :, None, None]

    def neighbours(quantity):
        east_west = with_halo(quantity, (("lon", 3),), 1, True)
        south_north = with_halo(quantity, (("lat", 2),), 1, False)
        top_row = quantity[:, :, -1, :]
        partner_row = fold_row(top_row, fold_partner)
        return (east_west, south_north, partner_row)

    def combine(quantity, east_flux, north_flux, vertical_part, uptake, forcing, sea):
        return sea * (
            quantity
            - (
                east_flux[..., 1:]
                - east_flux[..., :-1]
                + (north_flux[:, :, 1:, :] - north_flux[:, :, :-1, :])
                + vertical_part
            )
            - uptake
            + forcing
        )

    kept_states = [tracer_start]
    for _ in range(STEPS):
      advance_quantity = kept_states[-1]
      uptake = decay_rate * advance_quantity / jnp.sqrt(1.0 + advance_quantity * advance_quantity)
      divergence_east_west, divergence_south_north, divergence_partner_row = neighbours(
          advance_quantity
      )
      east_flux = (
          east_own * divergence_east_west[..., :-1] + east_next * divergence_east_west[..., 1:]
      )
      north_flux = (
          north_own * divergence_south_north[:, :, :-1, :]
          + north_next * divergence_south_north[:, :, 1:, :]
      )
      up_flux = up_own * advance_quantity[:, :-1] + up_next * advance_quantity[:, 1:]
      zero_level = jnp.zeros_like(advance_quantity[:, :1])
      vertical_part = jnp.concatenate([up_flux, zero_level], 1) - jnp.concatenate(
          [zero_level, up_flux], 1
      )
      main = combine(advance_quantity, east_flux, north_flux, vertical_part, uptake, source, ocean)
      divergence_top_row = advance_quantity[:, :, -1, :]
      fold_flux = fold_own * divergence_top_row + fold_next * divergence_partner_row
      top_north = north_flux[:, :, -2:, :].at[:, :, -1, :].add(fold_flux)
      top = combine(
          advance_quantity[:, :, -1:],
          east_flux[:, :, -1:],
          top_north,
          vertical_part[:, :, -1:],
          uptake[:, :, -1:],
          source[:, :, -1:],
          ocean[:, -1:],
      )
      kept_states.append(jnp.concatenate([main[:, :, :-1], top], axis=2))
    last_state = kept_states[-1]
    adjoint = ocean * (last_state - target)
    source_grad = ocean * adjoint
    for backward in range(STEPS - 1, 0, -1):
      current = kept_states[backward]
      weight = ocean * adjoint
      transposed_east_west, transposed_south_north, transposed_partner_row = neighbours(weight)
      east_diff = transposed_east_west[..., :-1] - transposed_east_west[..., 1:]
      north_diff = transposed_south_north[:, :, :-1, :] - transposed_south_north[:, :, 1:, :]
      up_diff = weight[:, :-1] - weight[:, 1:]
      result = east_own[..., 1:] * east_diff[..., 1:] + east_next[..., :-1] * east_diff[..., :-1]
      result = result + (
          north_own[:, 1:, :] * north_diff[:, :, 1:, :]
          + north_next[:, :-1, :] * north_diff[:, :, :-1, :]
      )
      transposed_zero_level = jnp.zeros_like(weight[:, :1])
      up_part = jnp.concatenate([up_own * up_diff, transposed_zero_level], 1) + jnp.concatenate(
          [transposed_zero_level, up_next * up_diff], 1
      )
      spread = 1.0 + current * current
      damping = decay_rate / (spread * jnp.sqrt(spread))
      main = weight - (result + up_part) - damping * weight
      top_result = result[:, :, -1:, :] + (
          fold_own * (weight[:, :, -1, :] - transposed_partner_row)
      )[:, :, None, :]
      top = (
          weight[:, :, -1:]
          - (top_result + up_part[:, :, -1:])
          - damping[:, :, -1:] * weight[:, :, -1:]
      )
      adjoint = jnp.concatenate([main[:, :, :-1], top], axis=2)
      source_grad = source_grad + ocean * adjoint
    squares = tree_sum(jnp.sum(source_grad * source_grad), ("lon", "lat"))
    return (source_grad, jnp.sqrt(squares))


def solution(mesh):
    return jax.shard_map(
        on_device,
        mesh=mesh,
        in_specs=(
            P(None, None, "lat", "lon"),
            P(None, None, "lat", "lon"),
            P(None, None, "lat", "lon"),
            P(None, "lat", "lon"),
            P(None, "lat", "lon"),
            P(None, "lat", "lon"),
            P(None, "lat", "lon"),
            P(None, "lat", "lon"),
            P(),
            P("lon"),
        ),
        out_specs=(P(None, None, "lat", "lon"), P()),
        check_vma=False,
    )
```

```python
import jax
import jax.numpy as jnp
from jax import lax
from jax.sharding import PartitionSpec as P

STEPS = 4


def with_halo(block, sides, width, periodic):
    for axis, dim in sides:
        count = lax.axis_size(axis)
        forward = [(i, i + 1) for i in range(count - 1)]
        if periodic:
            forward.append((count - 1, 0))
        backward = [(target, source) for source, target in forward]
        low = lax.ppermute(
            lax.slice_in_dim(block, block.shape[dim] - width, None, axis=dim), axis, forward
        )
        high = lax.ppermute(lax.slice_in_dim(block, 0, width, axis=dim), axis, backward)
        block = jnp.concatenate([low, block, high], axis=dim)
    return block


def fold_row(row, fold_partner):
    count = lax.axis_size("lon")
    width = row.shape[-1]
    here = lax.axis_index("lon")
    offset = (fold_partner[0] + width * here) % (width * count)
    turns = offset // width
    shift = offset % width
    flipped = row[..., ::-1]
    slots = jnp.arange(count).reshape((count,) + (1,) * row.ndim)
    wanted = (slots == (turns - here) % count) | (slots == (turns - here - 1) % count)
    sent = jnp.where(wanted, flipped[None], 0.0)
    got = lax.all_to_all(sent, "lon", 0, 0)
    first = lax.dynamic_index_in_dim(got, (turns - here) % count, 0, keepdims=False)
    second = lax.dynamic_index_in_dim(got, (turns - here - 1) % count, 0, keepdims=False)
    pair = jnp.concatenate([first, second], axis=-1)
    return lax.dynamic_slice_in_dim(pair, width - 1 - shift, width, axis=pair.ndim - 1)


def tree_sum(value, axes):
    count = 1
    for axis in axes:
        count *= lax.axis_size(axis)
    got = lax.all_to_all(jnp.broadcast_to(value, (count,)), axes, 0, 0)
    return jnp.sum(got)


def upwind_pair(velocity, mixing, face_sea):
    flow_rate = velocity * face_sea
    mixing_part = mixing * face_sea
    return (jnp.maximum(flow_rate, 0.0) + mixing_part, jnp.minimum(flow_rate, 0.0) - mixing_part)


def on_device(
    tracer_start,
    source,
    target,
    east_vel,
    north_vel,
    vertical_vel,
    diffusivity,
    sea_mask,
    reaction_rate,
    fold_partner,
):
    ocean = sea_mask.astype(jnp.float32)
    statics = jnp.stack([east_vel, north_vel, diffusivity, ocean])
    count_static = statics.shape[0]
    joined = jnp.concatenate([statics, tracer_start])
    wide_joined = with_halo(joined, (("lon", 3),), 1, True)
    tall_joined = with_halo(joined, (("lat", 2),), 1, False)
    wide_static = wide_joined[:count_static]
    tall_static = tall_joined[:count_static]
    start_east_west = wide_joined[count_static:]
    start_south_north = tall_joined[count_static:]
    west_cell = wide_static[..., :-1]
    east_cell = wide_static[..., 1:]
    east_own, east_next = upwind_pair(
        west_cell[0], 0.5 * (west_cell[2] + east_cell[2]), west_cell[3] * east_cell[3]
    )
    below_row = tall_static[:, :, :-1, :]
    above_row = tall_static[:, :, 1:, :]
    north_own, north_next = upwind_pair(
        below_row[1], 0.5 * (below_row[2] + above_row[2]), below_row[3] * above_row[3]
    )
    up_own, up_next = upwind_pair(
        vertical_vel[:-1], 0.5 * (diffusivity[:-1] + diffusivity[1:]), ocean[:-1] * ocean[1:]
    )
    top_static = jnp.stack([north_vel[:, -1, :], diffusivity[:, -1, :], ocean[:, -1, :]])
    top_joined = jnp.concatenate([top_static, tracer_start[:, :, -1, :]])
    across_joined = fold_row(top_joined, fold_partner)
    across = across_joined[: top_static.shape[0]]
    start_partner_row = across_joined[top_static.shape[0] :]
    north_top = (lax.axis_index("lat") == lax.axis_size("lat") - 1).astype(jnp.float32)
    fold_own, fold_next = upwind_pair(
        0.5 * (top_static[0] - across[0]),
        0.5 * (top_static[1] + across[1]),
        top_static[2] * across[2] * north_top,
    )
    decay_rate = reaction_rate[:, :, None, None]

    def neighbours(quantity):
        east_west = with_halo(quantity, (("lon", 3),), 1, True)
        south_north = with_halo(quantity, (("lat", 2),), 1, False)
        top_row = quantity[:, :, -1, :]
        partner_row = fold_row(top_row, fold_partner)
        return (east_west, south_north, partner_row)

    kept_states = [tracer_start]
    for repeat in range(STEPS):
        advance_quantity = kept_states[-1]
        uptake = decay_rate * advance_quantity / jnp.sqrt(1.0 + advance_quantity * advance_quantity)
        if repeat == 0:
            divergence_east_west = start_east_west
            divergence_south_north = start_south_north
            divergence_partner_row = start_partner_row
        else:
            divergence_east_west, divergence_south_north, divergence_partner_row = neighbours(
                advance_quantity
            )
        east_flux = (
            east_own * divergence_east_west[..., :-1] + east_next * divergence_east_west[..., 1:]
        )
        north_flux = (
            north_own * divergence_south_north[:, :, :-1, :]
            + north_next * divergence_south_north[:, :, 1:, :]
        )
        divergence_top_row = advance_quantity[:, :, -1, :]
        fold_flux = fold_own * divergence_top_row + fold_next * divergence_partner_row
        north_flux = north_flux.at[:, :, -1, :].add(fold_flux)
        up_flux = up_own * advance_quantity[:, :-1] + up_next * advance_quantity[:, 1:]
        zero_level = jnp.zeros_like(advance_quantity[:, :1])
        vertical_part = jnp.concatenate([up_flux, zero_level], 1) - jnp.concatenate(
            [zero_level, up_flux], 1
        )
        kept_states.append(
            ocean
            * (
                advance_quantity
                - (
                    east_flux[..., 1:]
                    - east_flux[..., :-1]
                    + (north_flux[:, :, 1:, :] - north_flux[:, :, :-1, :])
                    + vertical_part
                )
                - uptake
                + source
            )
        )
    last_state = kept_states[-1]
    adjoint = ocean * (last_state - target)
    source_grad = ocean * adjoint
    for backward in range(STEPS - 1, 0, -1):
        current = kept_states[backward]
        weight = ocean * adjoint
        transposed_east_west, transposed_south_north, transposed_partner_row = neighbours(weight)
        east_diff = transposed_east_west[..., :-1] - transposed_east_west[..., 1:]
        north_diff = transposed_south_north[:, :, :-1, :] - transposed_south_north[:, :, 1:, :]
        up_diff = weight[:, :-1] - weight[:, 1:]
        result = east_own[..., 1:] * east_diff[..., 1:] + east_next[..., :-1] * east_diff[..., :-1]
        result = result + (
            north_own[:, 1:, :] * north_diff[:, :, 1:, :]
            + north_next[:, :-1, :] * north_diff[:, :, :-1, :]
        )
        result = result.at[:, :, -1, :].add(
            fold_own * (weight[:, :, -1, :] - transposed_partner_row)
        )
        transposed_zero_level = jnp.zeros_like(weight[:, :1])
        result = result + (
            jnp.concatenate([up_own * up_diff, transposed_zero_level], 1)
            + jnp.concatenate([transposed_zero_level, up_next * up_diff], 1)
        )
        spread = 1.0 + current * current
        adjoint = weight - result - decay_rate / (spread * jnp.sqrt(spread)) * weight
        source_grad = source_grad + ocean * adjoint
    squares = tree_sum(jnp.sum(source_grad * source_grad), ("lon", "lat"))
    return (source_grad, jnp.sqrt(squares))


def solution(mesh):
    return jax.shard_map(
        on_device,
        mesh=mesh,
        in_specs=(
            P(None, None, "lat", "lon"),
            P(None, None, "lat", "lon"),
            P(None, None, "lat", "lon"),
            P(None, "lat", "lon"),
            P(None, "lat", "lon"),
            P(None, "lat", "lon"),
            P(None, "lat", "lon"),
            P(None, "lat", "lon"),
            P(),
            P("lon"),
        ),
        out_specs=(P(None, None, "lat", "lon"), P()),
        check_vma=False,
    )
```

```python
import jax
import jax.numpy as jnp
from jax import lax
from jax.sharding import PartitionSpec as P

STEPS = 4


def with_halo(block, sides, width, periodic):
    for axis, dim in sides:
        count = lax.axis_size(axis)
        forward = [(i, i + 1) for i in range(count - 1)]
        if periodic:
            forward.append((count - 1, 0))
        backward = [(target, source) for source, target in forward]
        low = lax.ppermute(
            lax.slice_in_dim(block, block.shape[dim] - width, None, axis=dim), axis, forward
        )
        high = lax.ppermute(lax.slice_in_dim(block, 0, width, axis=dim), axis, backward)
        block = jnp.concatenate([low, block, high], axis=dim)
    return block


def fold_row(row, fold_partner):
    count = lax.axis_size("lon")
    width = row.shape[-1]
    here = lax.axis_index("lon")
    offset = (fold_partner[0] + width * here) % (width * count)
    turns = offset // width
    shift = offset % width
    flipped = row[..., ::-1]
    slots = jnp.arange(count).reshape((count,) + (1,) * row.ndim)
    wanted = (slots == (turns - here) % count) | (slots == (turns - here - 1) % count)
    sent = jnp.where(wanted, flipped[None], 0.0)
    got = lax.all_to_all(sent, "lon", 0, 0)
    first = lax.dynamic_index_in_dim(got, (turns - here) % count, 0, keepdims=False)
    second = lax.dynamic_index_in_dim(got, (turns - here - 1) % count, 0, keepdims=False)
    pair = jnp.concatenate([first, second], axis=-1)
    return lax.dynamic_slice_in_dim(pair, width - 1 - shift, width, axis=pair.ndim - 1)


def tree_sum(value, axes):
    count = 1
    for axis in axes:
        count *= lax.axis_size(axis)
    got = lax.all_to_all(jnp.broadcast_to(value, (count,)), axes, 0, 0)
    return jnp.sum(got)


def upwind_pair(velocity, mixing, face_sea):
    flow_rate = velocity * face_sea
    mixing_part = mixing * face_sea
    return (jnp.maximum(flow_rate, 0.0) + mixing_part, jnp.minimum(flow_rate, 0.0) - mixing_part)


def on_device(
    tracer_start,
    source,
    target,
    east_vel,
    north_vel,
    vertical_vel,
    diffusivity,
    sea_mask,
    reaction_rate,
    fold_partner,
):
    ocean = sea_mask.astype(jnp.float32)
    statics = jnp.stack([east_vel, north_vel, diffusivity, ocean])
    count_static = statics.shape[0]
    joined = jnp.concatenate([statics, tracer_start])
    wide_joined = with_halo(joined, (("lon", 3),), 1, True)
    tall_joined = with_halo(joined, (("lat", 2),), 1, False)
    wide_static = wide_joined[:count_static]
    tall_static = tall_joined[:count_static]
    start_east_west = wide_joined[count_static:]
    start_south_north = tall_joined[count_static:]
    west_cell = wide_static[..., :-1]
    east_cell = wide_static[..., 1:]
    east_own, east_next = upwind_pair(
        west_cell[0], 0.5 * (west_cell[2] + east_cell[2]), west_cell[3] * east_cell[3]
    )
    below_row = tall_static[:, :, :-1, :]
    above_row = tall_static[:, :, 1:, :]
    north_own, north_next = upwind_pair(
        below_row[1], 0.5 * (below_row[2] + above_row[2]), below_row[3] * above_row[3]
    )
    up_own, up_next = upwind_pair(
        vertical_vel[:-1], 0.5 * (diffusivity[:-1] + diffusivity[1:]), ocean[:-1] * ocean[1:]
    )
    top_static = jnp.stack([north_vel[:, -1, :], diffusivity[:, -1, :], ocean[:, -1, :]])
    top_joined = jnp.concatenate([top_static, tracer_start[:, :, -1, :]])
    across_joined = fold_row(top_joined, fold_partner)
    across = across_joined[: top_static.shape[0]]
    start_partner_row = across_joined[top_static.shape[0] :]
    north_top = (lax.axis_index("lat") == lax.axis_size("lat") - 1).astype(jnp.float32)
    fold_own, fold_next = upwind_pair(
        0.5 * (top_static[0] - across[0]),
        0.5 * (top_static[1] + across[1]),
        top_static[2] * across[2] * north_top,
    )
    decay_rate = reaction_rate[:, :, None, None]

    def neighbours(quantity):
        east_west = with_halo(quantity, (("lon", 3),), 1, True)
        south_north = with_halo(quantity, (("lat", 2),), 1, False)
        top_row = quantity[:, :, -1, :]
        partner_row = fold_row(top_row, fold_partner)
        return (east_west, south_north, partner_row)

    def combine(quantity, east_flux, north_flux, vertical_part, uptake, forcing, sea):
        return sea * (
            quantity
            - (
                east_flux[..., 1:]
                - east_flux[..., :-1]
                + (north_flux[:, :, 1:, :] - north_flux[:, :, :-1, :])
                + vertical_part
            )
            - uptake
            + forcing
        )

    kept_states = [tracer_start]
    for repeat in range(STEPS):
        advance_quantity = kept_states[-1]
        uptake = decay_rate * advance_quantity / jnp.sqrt(1.0 + advance_quantity * advance_quantity)
        if repeat == 0:
            divergence_east_west = start_east_west
            divergence_south_north = start_south_north
            divergence_partner_row = start_partner_row
        else:
            divergence_east_west, divergence_south_north, divergence_partner_row = neighbours(
                advance_quantity
            )
        east_flux = (
            east_own * divergence_east_west[..., :-1] + east_next * divergence_east_west[..., 1:]
        )
        north_flux = (
            north_own * divergence_south_north[:, :, :-1, :]
            + north_next * divergence_south_north[:, :, 1:, :]
        )
        up_flux = up_own * advance_quantity[:, :-1] + up_next * advance_quantity[:, 1:]
        zero_level = jnp.zeros_like(advance_quantity[:, :1])
        vertical_part = jnp.concatenate([up_flux, zero_level], 1) - jnp.concatenate(
            [zero_level, up_flux], 1
        )
        main = combine(
            advance_quantity, east_flux, north_flux, vertical_part, uptake, source, ocean
        )
        divergence_top_row = advance_quantity[:, :, -1, :]
        fold_flux = fold_own * divergence_top_row + fold_next * divergence_partner_row
        top_north = north_flux[:, :, -2:, :].at[:, :, -1, :].add(fold_flux)
        top = combine(
            advance_quantity[:, :, -1:],
            east_flux[:, :, -1:],
            top_north,
            vertical_part[:, :, -1:],
            uptake[:, :, -1:],
            source[:, :, -1:],
            ocean[:, -1:],
        )
        kept_states.append(jnp.concatenate([main[:, :, :-1], top], axis=2))
    last_state = kept_states[-1]
    adjoint = ocean * (last_state - target)
    source_grad = ocean * adjoint
    for backward in range(STEPS - 1, 0, -1):
        current = kept_states[backward]
        weight = ocean * adjoint
        transposed_east_west, transposed_south_north, transposed_partner_row = neighbours(weight)
        east_diff = transposed_east_west[..., :-1] - transposed_east_west[..., 1:]
        north_diff = transposed_south_north[:, :, :-1, :] - transposed_south_north[:, :, 1:, :]
        up_diff = weight[:, :-1] - weight[:, 1:]
        result = east_own[..., 1:] * east_diff[..., 1:] + east_next[..., :-1] * east_diff[..., :-1]
        result = result + (
            north_own[:, 1:, :] * north_diff[:, :, 1:, :]
            + north_next[:, :-1, :] * north_diff[:, :, :-1, :]
        )
        transposed_zero_level = jnp.zeros_like(weight[:, :1])
        up_part = jnp.concatenate([up_own * up_diff, transposed_zero_level], 1) + jnp.concatenate(
            [transposed_zero_level, up_next * up_diff], 1
        )
        spread = 1.0 + current * current
        damping = decay_rate / (spread * jnp.sqrt(spread))
        main = weight - (result + up_part) - damping * weight
        top_result = result[:, :, -1:, :] + (
            fold_own * (weight[:, :, -1, :] - transposed_partner_row)
        )[:, :, None, :]
        top = (
            weight[:, :, -1:]
            - (top_result + up_part[:, :, -1:])
            - damping[:, :, -1:] * weight[:, :, -1:]
        )
        adjoint = jnp.concatenate([main[:, :, :-1], top], axis=2)
        source_grad = source_grad + ocean * adjoint
    squares = tree_sum(jnp.sum(source_grad * source_grad), ("lon", "lat"))
    return (source_grad, jnp.sqrt(squares))


def solution(mesh):
    return jax.shard_map(
        on_device,
        mesh=mesh,
        in_specs=(
            P(None, None, "lat", "lon"),
            P(None, None, "lat", "lon"),
            P(None, None, "lat", "lon"),
            P(None, "lat", "lon"),
            P(None, "lat", "lon"),
            P(None, "lat", "lon"),
            P(None, "lat", "lon"),
            P(None, "lat", "lon"),
            P(),
            P("lon"),
        ),
        out_specs=(P(None, None, "lat", "lon"), P()),
        check_vma=False,
    )
```

```python
import jax
import jax.numpy as jnp
from jax import lax
from jax.sharding import PartitionSpec as P

STEPS = 4


def with_halo(block, sides, width, periodic):
    for axis, dim in sides:
        count = lax.axis_size(axis)
        forward = [(i, i + 1) for i in range(count - 1)]
        if periodic:
            forward.append((count - 1, 0))
        backward = [(target, source) for source, target in forward]
        low = lax.ppermute(
            lax.slice_in_dim(block, block.shape[dim] - width, None, axis=dim), axis, forward
        )
        high = lax.ppermute(lax.slice_in_dim(block, 0, width, axis=dim), axis, backward)
        block = jnp.concatenate([low, block, high], axis=dim)
    return block


def fold_row(row, fold_partner):
    count = lax.axis_size("lon")
    width = row.shape[-1]
    here = lax.axis_index("lon")
    offset = (fold_partner[0] + width * here) % (width * count)
    turns = offset // width
    shift = offset % width

    def branch(k):
        def move(flipped):
            first = lax.ppermute(flipped, "lon", [((k - d) % count, d) for d in range(count)])
            second = lax.ppermute(flipped, "lon", [((k - d - 1) % count, d) for d in range(count)])
            return jnp.concatenate([first, second], axis=-1)

        return move

    pair = lax.switch(turns, [branch(k) for k in range(count)], row[..., ::-1])
    return lax.dynamic_slice_in_dim(pair, width - 1 - shift, width, axis=pair.ndim - 1)


def tree_sum(value, axes):
    count = 1
    for axis in axes:
        count *= lax.axis_size(axis)
    got = lax.all_to_all(jnp.broadcast_to(value, (count,)), axes, 0, 0)
    return jnp.sum(got)


def upwind_pair(velocity, mixing, face_sea):
    flow_rate = velocity * face_sea
    mixing_part = mixing * face_sea
    return (jnp.maximum(flow_rate, 0.0) + mixing_part, jnp.minimum(flow_rate, 0.0) - mixing_part)


def on_device(
    tracer_start,
    source,
    target,
    east_vel,
    north_vel,
    vertical_vel,
    diffusivity,
    sea_mask,
    reaction_rate,
    fold_partner,
):
    ocean = sea_mask.astype(jnp.float32)
    statics = jnp.stack([east_vel, north_vel, diffusivity, ocean])
    count_static = statics.shape[0]
    joined = jnp.concatenate([statics, tracer_start])
    wide_joined = with_halo(joined, (("lon", 3),), 1, True)
    tall_joined = with_halo(joined, (("lat", 2),), 1, False)
    wide_static = wide_joined[:count_static]
    tall_static = tall_joined[:count_static]
    start_east_west = wide_joined[count_static:]
    start_south_north = tall_joined[count_static:]
    west_cell = wide_static[..., :-1]
    east_cell = wide_static[..., 1:]
    east_own, east_next = upwind_pair(
        west_cell[0], 0.5 * (west_cell[2] + east_cell[2]), west_cell[3] * east_cell[3]
    )
    below_row = tall_static[:, :, :-1, :]
    above_row = tall_static[:, :, 1:, :]
    north_own, north_next = upwind_pair(
        below_row[1], 0.5 * (below_row[2] + above_row[2]), below_row[3] * above_row[3]
    )
    up_own, up_next = upwind_pair(
        vertical_vel[:-1], 0.5 * (diffusivity[:-1] + diffusivity[1:]), ocean[:-1] * ocean[1:]
    )
    top_static = jnp.stack([north_vel[:, -1, :], diffusivity[:, -1, :], ocean[:, -1, :]])
    top_joined = jnp.concatenate([top_static, tracer_start[:, :, -1, :]])
    across_joined = fold_row(top_joined, fold_partner)
    across = across_joined[: top_static.shape[0]]
    start_partner_row = across_joined[top_static.shape[0] :]
    north_top = (lax.axis_index("lat") == lax.axis_size("lat") - 1).astype(jnp.float32)
    fold_own, fold_next = upwind_pair(
        0.5 * (top_static[0] - across[0]),
        0.5 * (top_static[1] + across[1]),
        top_static[2] * across[2] * north_top,
    )
    decay_rate = reaction_rate[:, :, None, None]

    def neighbours(quantity):
        east_west = with_halo(quantity, (("lon", 3),), 1, True)
        south_north = with_halo(quantity, (("lat", 2),), 1, False)
        top_row = quantity[:, :, -1, :]
        partner_row = fold_row(top_row, fold_partner)
        return (east_west, south_north, partner_row)

    kept_states = [tracer_start]
    for repeat in range(STEPS):
        advance_quantity = kept_states[-1]
        uptake = decay_rate * advance_quantity / jnp.sqrt(1.0 + advance_quantity * advance_quantity)
        if repeat == 0:
            divergence_east_west = start_east_west
            divergence_south_north = start_south_north
            divergence_partner_row = start_partner_row
        else:
            divergence_east_west, divergence_south_north, divergence_partner_row = neighbours(
                advance_quantity
            )
        east_flux = (
            east_own * divergence_east_west[..., :-1] + east_next * divergence_east_west[..., 1:]
        )
        north_flux = (
            north_own * divergence_south_north[:, :, :-1, :]
            + north_next * divergence_south_north[:, :, 1:, :]
        )
        divergence_top_row = advance_quantity[:, :, -1, :]
        fold_flux = fold_own * divergence_top_row + fold_next * divergence_partner_row
        north_flux = north_flux.at[:, :, -1, :].add(fold_flux)
        up_flux = up_own * advance_quantity[:, :-1] + up_next * advance_quantity[:, 1:]
        zero_level = jnp.zeros_like(advance_quantity[:, :1])
        vertical_part = jnp.concatenate([up_flux, zero_level], 1) - jnp.concatenate(
            [zero_level, up_flux], 1
        )
        kept_states.append(
            ocean
            * (
                advance_quantity
                - (
                    east_flux[..., 1:]
                    - east_flux[..., :-1]
                    + (north_flux[:, :, 1:, :] - north_flux[:, :, :-1, :])
                    + vertical_part
                )
                - uptake
                + source
            )
        )
    last_state = kept_states[-1]
    adjoint = ocean * (last_state - target)
    source_grad = ocean * adjoint
    for backward in range(STEPS - 1, 0, -1):
        current = kept_states[backward]
        weight = ocean * adjoint
        transposed_east_west, transposed_south_north, transposed_partner_row = neighbours(weight)
        east_diff = transposed_east_west[..., :-1] - transposed_east_west[..., 1:]
        north_diff = transposed_south_north[:, :, :-1, :] - transposed_south_north[:, :, 1:, :]
        up_diff = weight[:, :-1] - weight[:, 1:]
        result = east_own[..., 1:] * east_diff[..., 1:] + east_next[..., :-1] * east_diff[..., :-1]
        result = result + (
            north_own[:, 1:, :] * north_diff[:, :, 1:, :]
            + north_next[:, :-1, :] * north_diff[:, :, :-1, :]
        )
        result = result.at[:, :, -1, :].add(
            fold_own * (weight[:, :, -1, :] - transposed_partner_row)
        )
        transposed_zero_level = jnp.zeros_like(weight[:, :1])
        result = result + (
            jnp.concatenate([up_own * up_diff, transposed_zero_level], 1)
            + jnp.concatenate([transposed_zero_level, up_next * up_diff], 1)
        )
        spread = 1.0 + current * current
        adjoint = weight - result - decay_rate / (spread * jnp.sqrt(spread)) * weight
        source_grad = source_grad + ocean * adjoint
    squares = tree_sum(jnp.sum(source_grad * source_grad), ("lon", "lat"))
    return (source_grad, jnp.sqrt(squares))


def solution(mesh):
    return jax.shard_map(
        on_device,
        mesh=mesh,
        in_specs=(
            P(None, None, "lat", "lon"),
            P(None, None, "lat", "lon"),
            P(None, None, "lat", "lon"),
            P(None, "lat", "lon"),
            P(None, "lat", "lon"),
            P(None, "lat", "lon"),
            P(None, "lat", "lon"),
            P(None, "lat", "lon"),
            P(),
            P("lon"),
        ),
        out_specs=(P(None, None, "lat", "lon"), P()),
        check_vma=False,
    )
```
